512 devices in a mesh: wall: 4 (over x_lo, core), span: 16 (over y, x_hi), stream: 8 (over z).
Axes of the slice: x: 4 (x_hi: 2, x_lo: 2; x = x_hi * 2 + x_lo), y: 8, z: 8, core: 2. Of those that a mesh axis runs over, the one named last changes fastest.
Arguments:
- right_side: float32 [16, 8, 8, 64, 320], P('span', 'stream', 'wall'), may hold values from -6 to 6
- old_values: float32 [16, 8, 8, 64, 320], P('span', 'stream', 'wall'), may hold values from -6 to 6
- element_library: float32 [8, 320], replicated, as said below
- wall_library: float32 [3, 320, 320], replicated, as said below
- face_library: float32 [4, 320, 320], replicated, may hold values from -0.15625 to 0.15625
- element_index: int32 [16, 8, 8], P('span', 'stream', 'wall'), may hold values from 0 to 7
- wall_faces: int32 [16, 8, 8, 2], P('span', 'stream', 'wall'), may hold values from 0 to 2, as said below
- face_index: int32 [16, 8, 8, 4], P('span', 'stream', 'wall'), may hold values from 0 to 3
Outputs:
- new_values: float32 [16, 8, 8, 64, 320], P('span', 'stream', 'wall')
The draws below stay inside these ranges and needn't reach their ends.
Inputs may be any that keep to these rules, and one draw needn't show every extreme that they name: On every line wall_faces[..., i, 1] equals wall_faces[..., i + 1, 0] for i < 7. `wall_library`: every block is symmetric positive definite. `element_library`: entries are positive.
All inputs are finite; a program needn't handle non-finite values.
Results may differ from the reference program's by a relative error of at most 0.0003.
Values sent between devices are 32-bit elements; how exact they have to be, the bound alone decides.
No kernel may reach another device: no remote copies, remote signals or barrier semaphores. Data moves between devices by JAX's collectives and lax.ppermute only.
A program may use at most 64 MiB of HBM per device.

```python
import math
import jax
import jax.numpy as jnp
from jax import lax

ELEMENT_UNKNOWNS = 320
NVEC = 64
NQ = 3
NN = 4
LIBRARY_ELEMENTS = 8
LINE = 8
NSPAN = 16
NFLOW = 8


wall_strength = 10.0


def draw_element_library(key, part):
    key_select, key_gradual, key_quick, key_sudden, key_rows_draw = jax.random.split(key, 5)
    share = 0.5
    slow_mask = jax.random.uniform(key_select, (LIBRARY_ELEMENTS, ELEMENT_UNKNOWNS), jnp.float32) < share
    slow_rate = jnp.exp(jax.random.uniform(key_gradual, (LIBRARY_ELEMENTS, ELEMENT_UNKNOWNS), jnp.float32, math.log(0.002), math.log(0.01)))
    fast_rate = jnp.exp(jax.random.uniform(key_quick, (LIBRARY_ELEMENTS, ELEMENT_UNKNOWNS), jnp.float32, math.log(1.0), math.log(10.0)))
    sudden_rate = jnp.exp(jax.random.uniform(key_sudden, (LIBRARY_ELEMENTS, ELEMENT_UNKNOWNS), jnp.float32, math.log(0.5), math.log(1.5)))
    sudden_row = jax.random.randint(key_rows_draw, (), 0, LIBRARY_ELEMENTS, dtype=jnp.int32)
    rate_values = jnp.where(slow_mask, slow_rate, fast_rate)
    library_row_list = jnp.arange(LIBRARY_ELEMENTS, dtype=jnp.int32)[:, None]
    return jnp.where(library_row_list == sudden_row, sudden_rate, rate_values)


def draw_wall_library(key, part):
    key_noise, key_diag = jax.random.split(key)
    spread = 0.1
    reach = 0.6
    raw = jax.random.uniform(key_noise, (NQ, ELEMENT_UNKNOWNS, ELEMENT_UNKNOWNS), jnp.float32, -1.0, 1.0)
    noise = (raw + jnp.swapaxes(raw, 1, 2)) * (0.5 * reach * wall_strength / math.sqrt(ELEMENT_UNKNOWNS))
    diagonal = wall_strength * jax.random.uniform(key_diag, (NQ, ELEMENT_UNKNOWNS), jnp.float32, 1.0 - spread, 1.0 + spread)
    return noise + diagonal[:, :, None] * jnp.eye(ELEMENT_UNKNOWNS, dtype=jnp.float32)[None]


def draw_wall_faces(key, part):
    faces = jax.random.randint(key, (NSPAN, NFLOW, LINE + 1), 0, NQ, dtype=jnp.int32)
    return jnp.stack([faces[:, :, :-1], faces[:, :, 1:]], axis=-1)


def set_ends(entries, own_key, smallest, high):
    longest = entries.shape.index(max(entries.shape))
    spots = []
    for shift in (0, 1):
        where = [jax.random.randint(jax.random.fold_in(own_key, axis), (), 0, length) for axis, length in enumerate(entries.shape)]
        where[longest] = (where[longest] + shift) % entries.shape[longest]
        spots.append(tuple(where))
    return entries.at[spots[0]].set(smallest).at[spots[1]].set(high)


def level_of(own_key, dims, cuts, least, largest):
    factor_of = 1.0
    for dim, shards_of in cuts:
        heights = jax.random.uniform(jax.random.fold_in(jax.random.fold_in(own_key, 6), dim), (shards_of,), jnp.float32, least / len(cuts), largest / len(cuts))
        factor_of = factor_of * jnp.repeat(jnp.exp(heights), dims[dim] // shards_of).reshape((-1,) + (1,) * (len(dims) - 1 - dim))
    return factor_of


def normal_values(key, dims, scale, most, cuts=(), held_as=jnp.bfloat16):
    drawn = jax.random.normal(key, dims, jnp.float32) * scale
    if len(cuts) > 0:
        drawn = level_of(key, dims, cuts, -0.22, 0.18) * drawn
    return jnp.clip(drawn, min=-most, max=most).astype(held_as)


def setup_inputs(seed: int = 0) -> dict:
    arg_keys = jax.random.split(jax.random.key(seed), 9)
    right_side = normal_values(arg_keys[0], (NSPAN, NFLOW, LINE, NVEC, ELEMENT_UNKNOWNS), 1.0, 6.0, ((0, 16), (1, 8), (2, 4)), jnp.float32)
    old_values = normal_values(arg_keys[1], (NSPAN, NFLOW, LINE, NVEC, ELEMENT_UNKNOWNS), 1.0, 6.0, ((0, 16), (1, 8), (2, 4)), jnp.float32)
    element_library = draw_element_library(jax.random.fold_in(arg_keys[8], 71), 0)
    wall_library = draw_wall_library(jax.random.fold_in(arg_keys[8], 71), 0)
    face_library = normal_values(arg_keys[4], (NN, ELEMENT_UNKNOWNS, ELEMENT_UNKNOWNS), (4 * ELEMENT_UNKNOWNS) ** -0.5, 0.15625, (), jnp.float32)
    element_index = set_ends(jax.random.randint(arg_keys[5], (NSPAN, NFLOW, LINE), 0, LIBRARY_ELEMENTS), jax.random.fold_in(arg_keys[5], 1), 0, LIBRARY_ELEMENTS - 1).astype(jnp.int32)
    wall_faces = draw_wall_faces(jax.random.fold_in(arg_keys[8], 71), 0)
    face_index = set_ends(jax.random.randint(arg_keys[7], (NSPAN, NFLOW, LINE, 4), 0, NN), jax.random.fold_in(arg_keys[7], 1), 0, NN - 1).astype(jnp.int32)
    return dict(right_side=right_side, old_values=old_values, element_library=element_library, wall_library=wall_library, face_library=face_library, element_index=element_index, wall_faces=wall_faces, face_index=face_index)


HIGHEST = lax.Precision.HIGHEST

def lower_solve(factor, values):
    return jax.scipy.linalg.solve_triangular(factor, values, lower=True)

def upper_solve(factor, values):
    return jax.scipy.linalg.solve_triangular(factor, values, lower=True, trans=1)

def solve_line(residual_t, element_rates, line_faces, wall_library):

    def pivot_of(rate_row, face_pair):
        return jnp.diag(rate_row) + wall_library[face_pair[0]] + wall_library[face_pair[1]]
    first_factor = jnp.linalg.cholesky(pivot_of(element_rates[0], line_faces[0]))

    def advance_one(carried_state, per_element):
        factor_prev, carried_prev = carried_state
        rate_row, face_pair, residual_row = per_element
        coupling = wall_library[face_pair[0]]
        scaled = lower_solve(factor_prev, coupling)
        reduced = lower_solve(factor_prev, carried_prev)
        pivot_now = pivot_of(rate_row, face_pair) - jnp.dot(scaled.T, scaled, precision=HIGHEST)
        carried = residual_row + jnp.dot(scaled.T, reduced, precision=HIGHEST)
        factor = jnp.linalg.cholesky(pivot_now)
        return ((factor, carried), (factor, carried))
    start_carry = (first_factor, residual_t[0])
    unused_state, (factors, carries) = lax.scan(advance_one, start_carry, (element_rates[1:], line_faces[1:], residual_t[1:]))
    factors = jnp.concatenate([first_factor[None], factors], axis=0)
    carries = jnp.concatenate([residual_t[:1], carries], axis=0)

    def retreat_one(term_next, per_element):
        factor, carried, face_pair = per_element
        solution = upper_solve(factor, lower_solve(factor, carried + term_next))
        return (jnp.dot(wall_library[face_pair[0]], solution, precision=HIGHEST), solution)
    unused_term, solutions = lax.scan(retreat_one, jnp.zeros_like(residual_t[0]), (factors, carries, line_faces), reverse=True)
    return solutions

def reference(right_side, old_values, element_library, wall_library, face_library, element_index, wall_faces, face_index):

    def one_line(line_number):
        span_pos = line_number // NFLOW
        flow_pos = line_number % NFLOW

        def neighbour(span_at, flow_at):
            return old_values[span_at % NSPAN, flow_at % NFLOW]
        near_rows = jnp.stack([neighbour(span_pos - 1, flow_pos), neighbour(span_pos + 1, flow_pos), neighbour(span_pos, flow_pos - 1), neighbour(span_pos, flow_pos + 1)], axis=1)
        blocks = face_library[face_index[span_pos, flow_pos]]
        coupled = jnp.einsum('edjk,edvk->ejv', blocks, near_rows, precision=HIGHEST)
        residual_t = jnp.swapaxes(right_side[span_pos, flow_pos], 1, 2) - coupled
        element_rates = element_library[element_index[span_pos, flow_pos]]
        solutions = solve_line(residual_t, element_rates, wall_faces[span_pos, flow_pos], wall_library)
        return jnp.swapaxes(solutions, 1, 2)
    lines = lax.map(one_line, jnp.arange(NSPAN * NFLOW, dtype=jnp.int32))
    return lines.reshape((NSPAN, NFLOW, LINE, NVEC, ELEMENT_UNKNOWNS))
```

```python
import jax
import jax.numpy as jnp
from jax import lax
from jax.sharding import PartitionSpec as P

HIGHEST = lax.Precision.HIGHEST


def padded_2(cells, sides, width):
    for axis, dim in sides:
        count = lax.axis_size(axis)
        head = lax.slice_in_dim(cells, 0, width, axis=dim)
        tail = lax.slice_in_dim(cells, cells.shape[dim] - width, cells.shape[dim], axis=dim)
        cells = jnp.concatenate(
            [
                lax.ppermute(tail, axis, [(i, (i + 1) % count) for i in range(count)]),
                cells,
                lax.ppermute(head, axis, [((i + 1) % count, i) for i in range(count)]),
            ],
            axis=dim,
        )
    return cells


def mm(spec, a, b):
    return jnp.einsum(spec, a, b, precision=HIGHEST)


def tr(a):
    return jnp.swapaxes(a, -1, -2)


def inverse_spd(blocks):
    factor = jnp.linalg.cholesky(blocks)
    eye = jnp.broadcast_to(jnp.eye(blocks.shape[-1], dtype=blocks.dtype), blocks.shape)
    factor_inv = lax.linalg.triangular_solve(factor, eye, left_side=True, lower=True)
    return mm("bki,bkj->bij", factor_inv, factor_inv)


def factor_line(diag, upper):
    levels = []
    while diag.shape[0] > 1:
        count = diag.shape[0]
        odd_count = count // 2
        has_right = [2 * j + 2 < count for j in range(odd_count)]
        right_count = sum(has_right)
        inv_odd = inverse_spd(diag[1::2])
        left = upper[0::2][:odd_count]
        right = upper[1::2][:right_count]
        to_left = mm("bij,bkj->bik", inv_odd, left)
        to_right = mm("bij,bjk->bik", inv_odd[:right_count], right)
        even = diag[0::2]
        even_count = even.shape[0]
        first = mm("bij,bjk->bik", left, to_left)
        even = even.at[:odd_count].add(-first)
        second = mm("bji,bjk->bik", right, to_right)
        even = even.at[1 : 1 + right_count].add(-second)
        next_upper = mm("bij,bjk->bik", left[: even_count - 1], to_right[: even_count - 1])
        levels.append((inv_odd, to_left, to_right))
        diag, upper = even, next_upper
    last_inv = inverse_spd(diag)
    return levels, last_inv


def solve_line(levels, last_inv, rhs):
    kept = []
    for inv_odd, to_left, to_right in levels:
        count = rhs.shape[0]
        odd = rhs[1::2]
        even = rhs[0::2]
        odd_count = odd.shape[0]
        right_count = to_right.shape[0]
        even = even.at[:odd_count].add(mm("bji,bjv->biv", to_left, odd))
        even = even.at[1 : 1 + right_count].add(mm("bji,bjv->biv", to_right, odd[:right_count]))
        kept.append((odd, count))
        rhs = even
    values = mm("bij,bjv->biv", last_inv, rhs)
    for (inv_odd, to_left, to_right), (odd, count) in zip(reversed(levels), reversed(kept)):
        right_count = to_right.shape[0]
        odd_values = mm("bij,bjv->biv", inv_odd, odd)
        odd_values = odd_values + mm("bij,bjv->biv", to_left, values[: odd.shape[0]])
        odd_values = odd_values.at[:right_count].add(
            mm("bij,bjv->biv", to_right, values[1 : 1 + right_count])
        )
        merged = jnp.zeros((count,) + values.shape[1:], values.dtype)
        merged = merged.at[0::2].set(values).at[1::2].set(odd_values)
        values = merged
    return values


def on_device(
    right_side,
    old_values,
    element_library,
    wall_library,
    face_library,
    element_index,
    wall_faces,
    face_index,
):
    local_side = right_side[0, 0]
    element_count = local_side.shape[0]
    indices = jnp.concatenate([element_index[0, 0][:, None], wall_faces[0, 0]], axis=1)
    line_indices = lax.all_gather(indices, "wall", axis=0, tiled=True)
    rates = element_library[line_indices[:, 0]]
    below = wall_library[line_indices[:, 1]]
    above = wall_library[line_indices[:, 2]]
    unknowns = rates.shape[1]
    diag = below + above + rates[:, :, None] * jnp.eye(unknowns, dtype=rates.dtype)[None]
    levels, last_inv = factor_line(diag, below[1:])

    padded = padded_2(old_values, (("span", 0), ("stream", 1)), 1)
    near_rows = jnp.stack([padded[0, 1], padded[2, 1], padded[1, 0], padded[1, 2]], axis=1)
    blocks = face_library[face_index[0, 0]]
    coupled = mm("edjk,edvk->ejv", blocks, near_rows)
    residual_t = jnp.swapaxes(local_side, 1, 2) - coupled
    line_residual = lax.all_gather(residual_t, "wall", axis=0, tiled=True)

    line_values = solve_line(levels, last_inv, line_residual)
    start = lax.axis_index("wall") * element_count
    own = lax.dynamic_slice_in_dim(line_values, start, element_count, axis=0)
    return jnp.swapaxes(own, 1, 2)[None, None]


def solution(mesh):
    placed = (
        P("span", "stream", "wall", None, None),
        P("span", "stream", "wall", None, None),
        P(),
        P(),
        P(),
        P("span", "stream", "wall"),
        P("span", "stream", "wall", None),
        P("span", "stream", "wall", None),
    )
    return jax.shard_map(
        on_device,
        mesh=mesh,
        in_specs=placed,
        out_specs=P("span", "stream", "wall", None, None),
        check_vma=False,
    )
```

```python
import jax
import jax.numpy as jnp
from jax import lax
from jax.sharding import PartitionSpec as P

HIGHEST = lax.Precision.HIGHEST


def padded_2(cells, sides, width):
    for axis, dim in sides:
        count = lax.axis_size(axis)
        head = lax.slice_in_dim(cells, 0, width, axis=dim)
        tail = lax.slice_in_dim(cells, cells.shape[dim] - width, cells.shape[dim], axis=dim)
        cells = jnp.concatenate(
            [
                lax.ppermute(tail, axis, [(i, (i + 1) % count) for i in range(count)]),
                cells,
                lax.ppermute(head, axis, [((i + 1) % count, i) for i in range(count)]),
            ],
            axis=dim,
        )
    return cells


def mm(spec, a, b):
    return jnp.einsum(spec, a, b, precision=HIGHEST)


def tr(a):
    return jnp.swapaxes(a, -1, -2)


def inverse_spd(block):
    factor = jnp.linalg.cholesky(block)
    eye = jnp.eye(block.shape[-1], dtype=block.dtype)
    factor_inv = lax.linalg.triangular_solve(factor, eye, left_side=True, lower=True)
    return mm("ki,kj->ij", factor_inv, factor_inv)


def pairs_of(sources, shift, count):
    return [(v, v + shift) for v in sources if 0 <= v + shift < count]


def on_device(
    right_side,
    old_values,
    element_library,
    wall_library,
    face_library,
    element_index,
    wall_faces,
    face_index,
):
    local_side = right_side[0, 0]
    assert local_side.shape[0] == 2
    wall_count = lax.axis_size("wall")
    position = lax.axis_index("wall")
    own_index = element_index[0, 0]
    own_faces = wall_faces[0, 0]
    rates = element_library[own_index]
    below = wall_library[own_faces[:, 0]]
    above = wall_library[own_faces[:, 1]]
    unknowns = rates.shape[1]
    eye = jnp.eye(unknowns, dtype=rates.dtype)
    diag_even = below[0] + above[0] + rates[0][:, None] * eye
    diag_odd = below[1] + above[1] + rates[1][:, None] * eye
    couple_in = below[1]
    couple_out = above[1]

    odd_inv = inverse_spd(diag_odd)

    padded = padded_2(old_values, (("span", 0), ("stream", 1)), 1)
    near_rows = jnp.stack([padded[0, 1], padded[2, 1], padded[1, 0], padded[1, 2]], axis=1)
    blocks = face_library[face_index[0, 0]]
    coupled = mm("edjk,edvk->ejv", blocks, near_rows)
    residual_t = jnp.swapaxes(local_side, 1, 2) - coupled
    odd_inv, residual_t = lax.optimization_barrier((odd_inv, residual_t))
    rhs_even = residual_t[0]
    rhs_odd = residual_t[1]

    odd_left = mm("ij,kj->ik", odd_inv, couple_in)
    odd_right = mm("ij,jk->ik", odd_inv, couple_out)
    to_left = mm("ij,jk->ik", couple_in, odd_left)
    to_right = mm("ji,jk->ik", couple_out, odd_right)
    coupling = mm("ij,jk->ik", couple_in, odd_right)
    coupling = jnp.where(position < wall_count - 1, coupling, jnp.zeros_like(coupling))
    rhs_left = mm("ji,jv->iv", odd_left, rhs_odd)
    rhs_right = mm("ji,jv->iv", odd_right, rhs_odd)
    from_left = lax.ppermute(
        (to_right, coupling, rhs_right), "wall", pairs_of(range(wall_count), 1, wall_count)
    )
    diag = diag_even - to_left - from_left[0]
    upper_right = coupling
    upper_left = from_left[1]
    rhs = rhs_even + rhs_left + from_left[2]

    levels = []
    stride = 1
    while stride < wall_count:
        senders = [v for v in range(wall_count) if v % (2 * stride) == stride]
        inv = inverse_spd(diag)
        left = mm("ij,kj->ik", inv, upper_left)
        right = mm("ij,jk->ik", inv, upper_right)
        to_left = mm("ij,jk->ik", upper_left, left)
        to_right = mm("ji,jk->ik", upper_right, right)
        coupling = mm("ij,jk->ik", upper_left, right)
        rhs_left = mm("ji,jv->iv", left, rhs)
        rhs_right = mm("ji,jv->iv", right, rhs)
        from_right = lax.ppermute(
            (to_left, coupling, rhs_left), "wall", pairs_of(senders, -stride, wall_count)
        )
        from_left = lax.ppermute(
            (to_right, coupling, rhs_right), "wall", pairs_of(senders, stride, wall_count)
        )
        levels.append((inv, left, right, rhs, stride, senders))
        diag = diag - from_right[0] - from_left[0]
        upper_right = from_right[1]
        upper_left = from_left[1]
        rhs = rhs + from_right[2] + from_left[2]
        stride *= 2

    values = mm("ij,jv->iv", inverse_spd(diag), rhs)
    for inv, left, right, level_rhs, stride, senders in reversed(levels):
        from_left = lax.ppermute(values, "wall", pairs_of([v - stride for v in senders], stride, wall_count))
        from_right = lax.ppermute(
            values, "wall", [(v + stride, v) for v in senders if v + stride < wall_count]
        )
        solved = (
            mm("ij,jv->iv", inv, level_rhs)
            + mm("ij,jv->iv", left, from_left)
            + mm("ij,jv->iv", right, from_right)
        )
        values = jnp.where(position % (2 * stride) == stride, solved, values)

    next_values = lax.ppermute(values, "wall", pairs_of(range(1, wall_count), -1, wall_count))
    odd_values = (
        mm("ij,jv->iv", odd_inv, rhs_odd)
        + mm("ij,jv->iv", odd_left, values)
        + mm("ij,jv->iv", odd_right, next_values)
    )
    own = jnp.stack([values, odd_values], axis=0)
    return jnp.swapaxes(own, 1, 2)[None, None]


def solution(mesh):
    placed = (
        P("span", "stream", "wall", None, None),
        P("span", "stream", "wall", None, None),
        P(),
        P(),
        P(),
        P("span", "stream", "wall"),
        P("span", "stream", "wall", None),
        P("span", "stream", "wall", None),
    )
    return jax.shard_map(
        on_device,
        mesh=mesh,
        in_specs=placed,
        out_specs=P("span", "stream", "wall", None, None),
        check_vma=False,
    )
```

```python
import jax
import jax.numpy as jnp
from jax import lax
from jax.experimental import pallas as pl
from jax.experimental.pallas import tpu as pltpu
from jax.sharding import PartitionSpec as P

HIGHEST = lax.Precision.HIGHEST


def shifted(cells, axis, by):
    count = lax.axis_size(axis)
    return lax.ppermute(cells, axis, [(i, (i + by) % count) for i in range(count)])


def mm(spec, a, b):
    return jnp.einsum(spec, a, b, precision=HIGHEST)


PANEL = 128


def panel_inverse(block):
    size = block.shape[0]
    rows = lax.broadcasted_iota(jnp.int32, (size, size), 0)
    cols = lax.broadcasted_iota(jnp.int32, (size, size), 1)
    row_ids = lax.broadcasted_iota(jnp.int32, (size, 1), 0)
    col_ids = lax.broadcasted_iota(jnp.int32, (1, size), 1)

    def step(k, current):
        on_row = rows == k
        on_col = cols == k
        row_k = jnp.sum(jnp.where(on_row, current, 0.0), axis=0, keepdims=True)
        col_k = jnp.sum(jnp.where(on_col, current, 0.0), axis=1, keepdims=True)
        pivot = jnp.sum(jnp.where(col_ids == k, row_k, 0.0), axis=1, keepdims=True)
        scaled = jnp.where(col_ids == k, 1.0, row_k) / pivot
        factor = jnp.where(row_ids == k, 0.0, col_k)
        current = jnp.where(on_col, 0.0, current) - factor * scaled
        return jnp.where(on_row, scaled, current)

    return lax.fori_loop(0, size, step, block)


def inverse_kernel(a_ref, o_ref):
    size = a_ref.shape[0]
    o_ref[...] = a_ref[...]
    row_ids = lax.broadcasted_iota(jnp.int32, (size, PANEL), 0)
    col_ids = lax.broadcasted_iota(jnp.int32, (PANEL, size), 1)
    lane_rows = lax.broadcasted_iota(jnp.int32, (PANEL, size), 0)
    for p in range(size // PANEL):
        part = slice(p * PANEL, (p + 1) * PANEL)
        inv = panel_inverse(o_ref[part, part])
        rows = o_ref[part, :]
        rows = jnp.where(
            (col_ids >= p * PANEL) & (col_ids < (p + 1) * PANEL),
            (col_ids - p * PANEL == lane_rows).astype(jnp.float32),
            rows,
        )
        new_rows = jnp.dot(inv, rows, precision=HIGHEST, preferred_element_type=jnp.float32)
        col = o_ref[:, part]
        col = jnp.where((row_ids >= p * PANEL) & (row_ids < (p + 1) * PANEL), 0.0, col)
        o_ref[:, part] = jnp.zeros((size, PANEL), jnp.float32)
        o_ref[...] = o_ref[...] - jnp.dot(col, new_rows, precision=HIGHEST, preferred_element_type=jnp.float32)
        o_ref[part, :] = new_rows


def inverse_spd(block):
    size = block.shape[-1]
    padded_size = -(-size // PANEL) * PANEL
    padded = jnp.pad(block, ((0, padded_size - size), (0, padded_size - size)))
    extra = (jnp.arange(padded_size) >= size).astype(block.dtype)
    padded = padded + jnp.diag(extra)
    out = pl.pallas_call(
        inverse_kernel,
        out_shape=jax.ShapeDtypeStruct((padded_size, padded_size), jnp.float32),
        in_specs=[pl.BlockSpec(memory_space=pltpu.VMEM)],
        out_specs=pl.BlockSpec(memory_space=pltpu.VMEM),
    )(padded)
    return out[:size, :size]


def pairs_of(sources, shift, count):
    return [(v, v + shift) for v in sources if 0 <= v + shift < count]


def on_device(
    right_side,
    old_values,
    element_library,
    wall_library,
    face_library,
    element_index,
    wall_faces,
    face_index,
):
    local_side = right_side[0, 0]
    assert local_side.shape[0] == 2
    wall_count = lax.axis_size("wall")
    position = lax.axis_index("wall")
    own_index = element_index[0, 0]
    own_faces = wall_faces[0, 0]
    rates = element_library[own_index]
    below = wall_library[own_faces[:, 0]]
    above = wall_library[own_faces[:, 1]]
    unknowns = rates.shape[1]
    eye = jnp.eye(unknowns, dtype=rates.dtype)
    diag_even = below[0] + above[0] + rates[0][:, None] * eye
    diag_odd = below[1] + above[1] + rates[1][:, None] * eye
    couple_in = below[1]
    couple_out = above[1]

    odd_inv = inverse_spd(diag_odd)

    near_rows = jnp.stack(
        [
            shifted(old_values, "span", 1),
            shifted(old_values, "span", -1),
            shifted(old_values, "stream", 1),
            shifted(old_values, "stream", -1),
        ],
        axis=3,
    )[0, 0]
    blocks = face_library[face_index[0, 0]]
    coupled = mm("edjk,edvk->ejv", blocks, near_rows)
    residual_t = jnp.swapaxes(local_side, 1, 2) - coupled
    odd_inv, residual_t = lax.optimization_barrier((odd_inv, residual_t))
    rhs_even = residual_t[0]
    rhs_odd = residual_t[1]

    odd_left = mm("ij,kj->ik", odd_inv, couple_in)
    odd_right = mm("ij,jk->ik", odd_inv, couple_out)
    to_left = mm("ij,jk->ik", couple_in, odd_left)
    to_right = mm("ji,jk->ik", couple_out, odd_right)
    coupling = mm("ij,jk->ik", couple_in, odd_right)
    coupling = jnp.where(position < wall_count - 1, coupling, jnp.zeros_like(coupling))
    rhs_left = mm("ji,jv->iv", odd_left, rhs_odd)
    rhs_right = mm("ji,jv->iv", odd_right, rhs_odd)
    from_left = lax.ppermute(
        (to_right, coupling, rhs_right), "wall", pairs_of(range(wall_count), 1, wall_count)
    )
    diag = diag_even - to_left - from_left[0]
    upper_right = coupling
    upper_left = from_left[1]
    rhs = rhs_even + rhs_left + from_left[2]

    levels = []
    stride = 1
    while stride < wall_count:
        senders = [v for v in range(wall_count) if v % (2 * stride) == stride]
        inv = inverse_spd(diag)
        left = mm("ij,kj->ik", inv, upper_left)
        right = mm("ij,jk->ik", inv, upper_right)
        to_left = mm("ij,jk->ik", upper_left, left)
        to_right = mm("ji,jk->ik", upper_right, right)
        coupling = mm("ij,jk->ik", upper_left, right)
        rhs_left = mm("ji,jv->iv", left, rhs)
        rhs_right = mm("ji,jv->iv", right, rhs)
        from_right = lax.ppermute(
            (to_left, coupling, rhs_left), "wall", pairs_of(senders, -stride, wall_count)
        )
        from_left = lax.ppermute(
            (to_right, coupling, rhs_right), "wall", pairs_of(senders, stride, wall_count)
        )
        levels.append((inv, left, right, rhs, stride, senders))
        diag = diag - from_right[0] - from_left[0]
        upper_right = from_right[1]
        upper_left = from_left[1]
        rhs = rhs + from_right[2] + from_left[2]
        stride *= 2

    values = mm("ij,jv->iv", inverse_spd(diag), rhs)
    for inv, left, right, level_rhs, stride, senders in reversed(levels):
        from_left = lax.ppermute(values, "wall", pairs_of([v - stride for v in senders], stride, wall_count))
        from_right = lax.ppermute(
            values, "wall", [(v + stride, v) for v in senders if v + stride < wall_count]
        )
        solved = (
            mm("ij,jv->iv", inv, level_rhs)
            + mm("ij,jv->iv", left, from_left)
            + mm("ij,jv->iv", right, from_right)
        )
        values = jnp.where(position % (2 * stride) == stride, solved, values)

    next_values = lax.ppermute(values, "wall", pairs_of(range(1, wall_count), -1, wall_count))
    odd_values = (
        mm("ij,jv->iv", odd_inv, rhs_odd)
        + mm("ij,jv->iv", odd_left, values)
        + mm("ij,jv->iv", odd_right, next_values)
    )
    own = jnp.stack([values, odd_values], axis=0)
    return jnp.swapaxes(own, 1, 2)[None, None]


def solution(mesh):
    placed = (
        P("span", "stream", "wall", None, None),
        P("span", "stream", "wall", None, None),
        P(),
        P(),
        P(),
        P("span", "stream", "wall"),
        P("span", "stream", "wall", None),
        P("span", "stream", "wall", None),
    )
    return jax.shard_map(
        on_device,
        mesh=mesh,
        in_specs=placed,
        out_specs=P("span", "stream", "wall", None, None),
        check_vma=False,
    )
```

```python
import jax
import jax.numpy as jnp
from jax import lax
from jax.experimental import pallas as pl
from jax.experimental.pallas import tpu as pltpu
from jax.sharding import PartitionSpec as P

HIGHEST = lax.Precision.HIGHEST


def shifted(cells, axis, by):
    count = lax.axis_size(axis)
    return lax.ppermute(cells, axis, [(i, (i + by) % count) for i in range(count)])


def mm(spec, a, b):
    return jnp.einsum(spec, a, b, precision=HIGHEST)


PANEL = 128


def panel_inverse(block):
    size = block.shape[0]
    rows = lax.broadcasted_iota(jnp.int32, (size, size), 0)
    cols = lax.broadcasted_iota(jnp.int32, (size, size), 1)
    row_ids = lax.broadcasted_iota(jnp.int32, (size, 1), 0)
    col_ids = lax.broadcasted_iota(jnp.int32, (1, size), 1)

    def step(k, current):
        on_row = rows == k
        on_col = cols == k
        row_k = jnp.sum(jnp.where(on_row, current, 0.0), axis=0, keepdims=True)
        col_k = jnp.sum(jnp.where(on_col, current, 0.0), axis=1, keepdims=True)
        pivot = jnp.sum(jnp.where(col_ids == k, row_k, 0.0), axis=1, keepdims=True)
        scaled = jnp.where(col_ids == k, 1.0, row_k) / pivot
        factor = jnp.where(row_ids == k, 0.0, col_k)
        current = jnp.where(on_col, 0.0, current) - factor * scaled
        return jnp.where(on_row, scaled, current)

    return lax.fori_loop(0, size, step, block)


def inverse_kernel(a_ref, o_ref):
    size = a_ref.shape[0]
    o_ref[...] = a_ref[...]
    row_ids = lax.broadcasted_iota(jnp.int32, (size, PANEL), 0)
    col_ids = lax.broadcasted_iota(jnp.int32, (PANEL, size), 1)
    lane_rows = lax.broadcasted_iota(jnp.int32, (PANEL, size), 0)
    for p in range(size // PANEL):
        part = slice(p * PANEL, (p + 1) * PANEL)
        inv = panel_inverse(o_ref[part, part])
        rows = o_ref[part, :]
        rows = jnp.where(
            (col_ids >= p * PANEL) & (col_ids < (p + 1) * PANEL),
            (col_ids - p * PANEL == lane_rows).astype(jnp.float32),
            rows,
        )
        new_rows = jnp.dot(inv, rows, precision=HIGHEST, preferred_element_type=jnp.float32)
        col = o_ref[:, part]
        col = jnp.where((row_ids >= p * PANEL) & (row_ids < (p + 1) * PANEL), 0.0, col)
        o_ref[:, part] = jnp.zeros((size, PANEL), jnp.float32)
        o_ref[...] = o_ref[...] - jnp.dot(col, new_rows, precision=HIGHEST, preferred_element_type=jnp.float32)
        o_ref[part, :] = new_rows


def inverse_spd(block):
    size = block.shape[-1]
    padded_size = -(-size // PANEL) * PANEL
    padded = jnp.pad(block, ((0, padded_size - size), (0, padded_size - size)))
    extra = (jnp.arange(padded_size) >= size).astype(block.dtype)
    padded = padded + jnp.diag(extra)
    out = pl.pallas_call(
        inverse_kernel,
        out_shape=jax.ShapeDtypeStruct((padded_size, padded_size), jnp.float32),
        in_specs=[pl.BlockSpec(memory_space=pltpu.VMEM)],
        out_specs=pl.BlockSpec(memory_space=pltpu.VMEM),
    )(padded)
    return out[:size, :size]


def pairs_of(sources, shift, count):
    return [(v, v + shift) for v in sources if 0 <= v + shift < count]


def on_device(
    right_side,
    old_values,
    element_library,
    wall_library,
    face_library,
    element_index,
    wall_faces,
    face_index,
):
    local_side = right_side[0, 0]
    assert local_side.shape[0] == 2
    wall_count = lax.axis_size("wall")
    position = lax.axis_index("wall")
    own_index = element_index[0, 0]
    own_faces = wall_faces[0, 0]
    rates = element_library[own_index]
    below = wall_library[own_faces[:, 0]]
    above = wall_library[own_faces[:, 1]]
    unknowns = rates.shape[1]
    eye = jnp.eye(unknowns, dtype=rates.dtype)
    diag_even = below[0] + above[0] + rates[0][:, None] * eye
    diag_odd = below[1] + above[1] + rates[1][:, None] * eye
    couple_in = below[1]
    couple_out = above[1]

    odd_inv = inverse_spd(diag_odd)

    near_rows = jnp.stack(
        [
            shifted(old_values, "span", 1),
            shifted(old_values, "span", -1),
            shifted(old_values, "stream", 1),
            shifted(old_values, "stream", -1),
        ],
        axis=3,
    )[0, 0]
    blocks = face_library[face_index[0, 0]]
    coupled = mm("edjk,edvk->ejv", blocks, near_rows)
    residual_t = jnp.swapaxes(local_side, 1, 2) - coupled
    odd_inv, residual_t = lax.optimization_barrier((odd_inv, residual_t))
    rhs_even = residual_t[0]
    rhs_odd = residual_t[1]

    odd_left = mm("ij,kj->ik", odd_inv, couple_in)
    odd_right = mm("ij,jk->ik", odd_inv, couple_out)
    to_left = mm("ij,jk->ik", couple_in, odd_left)
    to_right = mm("ji,jk->ik", couple_out, odd_right)
    coupling = mm("ij,jk->ik", couple_in, odd_right)
    coupling = jnp.where(position < wall_count - 1, coupling, jnp.zeros_like(coupling))
    rhs_left = mm("ji,jv->iv", odd_left, rhs_odd)
    rhs_right = mm("ji,jv->iv", odd_right, rhs_odd)
    from_left = lax.ppermute(
        (to_right, coupling, rhs_right), "wall", pairs_of(range(wall_count), 1, wall_count)
    )
    diag = diag_even - to_left - from_left[0]
    upper_right = coupling
    upper_left = from_left[1]
    rhs = rhs_even + rhs_left + from_left[2]

    stride = 1
    while stride < wall_count:
        inv = inverse_spd(diag)
        left = mm("ij,kj->ik", inv, upper_left)
        right = mm("ij,jk->ik", inv, upper_right)
        to_left = mm("ij,jk->ik", upper_left, left)
        to_right = mm("ji,jk->ik", upper_right, right)
        coupling = mm("ij,jk->ik", upper_left, right)
        rhs_left = mm("ji,jv->iv", left, rhs)
        rhs_right = mm("ji,jv->iv", right, rhs)
        from_right = lax.ppermute(
            (to_left, coupling, rhs_left), "wall", pairs_of(range(wall_count), -stride, wall_count)
        )
        from_left = lax.ppermute(
            (to_right, coupling, rhs_right), "wall", pairs_of(range(wall_count), stride, wall_count)
        )
        diag = diag - from_right[0] - from_left[0]
        upper_right = from_right[1]
        upper_left = from_left[1]
        rhs = rhs + from_right[2] + from_left[2]
        stride *= 2

    values = mm("ij,jv->iv", inverse_spd(diag), rhs)

    next_values = lax.ppermute(values, "wall", pairs_of(range(1, wall_count), -1, wall_count))
    odd_values = (
        mm("ij,jv->iv", odd_inv, rhs_odd)
        + mm("ij,jv->iv", odd_left, values)
        + mm("ij,jv->iv", odd_right, next_values)
    )
    own = jnp.stack([values, odd_values], axis=0)
    return jnp.swapaxes(own, 1, 2)[None, None]


def solution(mesh):
    placed = (
        P("span", "stream", "wall", None, None),
        P("span", "stream", "wall", None, None),
        P(),
        P(),
        P(),
        P("span", "stream", "wall"),
        P("span", "stream", "wall", None),
        P("span", "stream", "wall", None),
    )
    return jax.shard_map(
        on_device,
        mesh=mesh,
        in_specs=placed,
        out_specs=P("span", "stream", "wall", None, None),
        check_vma=False,
    )
```

```python
import jax
import jax.numpy as jnp
from jax import lax
from jax.experimental import pallas as pl
from jax.experimental.pallas import tpu as pltpu
from jax.sharding import PartitionSpec as P

HIGHEST = lax.Precision.HIGHEST


def shifted(cells, axis, by):
    count = lax.axis_size(axis)
    return lax.ppermute(cells, axis, [(i, (i + by) % count) for i in range(count)])


def mm(spec, a, b):
    return jnp.einsum(spec, a, b, precision=HIGHEST)


PANEL = 128


def panel_inverse(block, scratch):
    size = block.shape[0]
    rows = lax.broadcasted_iota(jnp.int32, (size, size), 0)
    cols = lax.broadcasted_iota(jnp.int32, (size, size), 1)
    row_ids = lax.broadcasted_iota(jnp.int32, (size, 1), 0)
    col_ids = lax.broadcasted_iota(jnp.int32, (1, size), 1)
    scratch[...] = block

    def step(k, carry):
        current = scratch[...]
        row_k = scratch[pl.ds(k, 1), :]
        on_col = cols == k
        col_k = jnp.sum(jnp.where(on_col, current, 0.0), axis=1, keepdims=True)
        pivot = jnp.sum(jnp.where(col_ids == k, row_k, 0.0), axis=1, keepdims=True)
        scaled = jnp.where(col_ids == k, 1.0, row_k) / pivot
        factor = jnp.where(row_ids == k, 0.0, col_k)
        current = jnp.where(on_col, 0.0, current) - factor * scaled
        scratch[...] = jnp.where(rows == k, scaled, current)
        return carry

    lax.fori_loop(0, size, step, 0)
    return scratch[...]


def inverse_kernel(a_ref, o_ref, scratch):
    size = a_ref.shape[0]
    o_ref[...] = a_ref[...]
    row_ids = lax.broadcasted_iota(jnp.int32, (size, PANEL), 0)
    col_ids = lax.broadcasted_iota(jnp.int32, (PANEL, size), 1)
    lane_rows = lax.broadcasted_iota(jnp.int32, (PANEL, size), 0)
    for p in range(size // PANEL):
        part = slice(p * PANEL, (p + 1) * PANEL)
        inv = panel_inverse(o_ref[part, part], scratch)
        rows = o_ref[part, :]
        rows = jnp.where(
            (col_ids >= p * PANEL) & (col_ids < (p + 1) * PANEL),
            (col_ids - p * PANEL == lane_rows).astype(jnp.float32),
            rows,
        )
        new_rows = jnp.dot(inv, rows, precision=HIGHEST, preferred_element_type=jnp.float32)
        col = o_ref[:, part]
        col = jnp.where((row_ids >= p * PANEL) & (row_ids < (p + 1) * PANEL), 0.0, col)
        o_ref[:, part] = jnp.zeros((size, PANEL), jnp.float32)
        o_ref[...] = o_ref[...] - jnp.dot(col, new_rows, precision=HIGHEST, preferred_element_type=jnp.float32)
        o_ref[part, :] = new_rows


def inverse_spd(block):
    size = block.shape[-1]
    padded_size = -(-size // PANEL) * PANEL
    padded = jnp.pad(block, ((0, padded_size - size), (0, padded_size - size)))
    extra = (jnp.arange(padded_size) >= size).astype(block.dtype)
    padded = padded + jnp.diag(extra)
    out = pl.pallas_call(
        inverse_kernel,
        out_shape=jax.ShapeDtypeStruct((padded_size, padded_size), jnp.float32),
        in_specs=[pl.BlockSpec(memory_space=pltpu.VMEM)],
        out_specs=pl.BlockSpec(memory_space=pltpu.VMEM),
        scratch_shapes=[pltpu.VMEM((PANEL, PANEL), jnp.float32)],
    )(padded)
    return out[:size, :size]


def unpack(packed, unknowns):
    return packed[:, :unknowns], packed[:, unknowns : 2 * unknowns], packed[:, 2 * unknowns :]


def pairs_of(sources, shift, count):
    return [(v, v + shift) for v in sources if 0 <= v + shift < count]


def on_device(
    right_side,
    old_values,
    element_library,
    wall_library,
    face_library,
    element_index,
    wall_faces,
    face_index,
):
    local_side = right_side[0, 0]
    assert local_side.shape[0] == 2
    wall_count = lax.axis_size("wall")
    position = lax.axis_index("wall")
    own_index = element_index[0, 0]
    own_faces = wall_faces[0, 0]
    rates = element_library[own_index]
    below = wall_library[own_faces[:, 0]]
    above = wall_library[own_faces[:, 1]]
    unknowns = rates.shape[1]
    eye = jnp.eye(unknowns, dtype=rates.dtype)
    diag_even = below[0] + above[0] + rates[0][:, None] * eye
    diag_odd = below[1] + above[1] + rates[1][:, None] * eye
    couple_in = below[1]
    couple_out = above[1]

    odd_inv = inverse_spd(diag_odd)

    near_rows = jnp.stack(
        [
            shifted(old_values, "span", 1),
            shifted(old_values, "span", -1),
            shifted(old_values, "stream", 1),
            shifted(old_values, "stream", -1),
        ],
        axis=3,
    )[0, 0]
    blocks = face_library[face_index[0, 0]]
    coupled = mm("edjk,edvk->ejv", blocks, near_rows)
    residual_t = jnp.swapaxes(local_side, 1, 2) - coupled
    odd_inv, residual_t = lax.optimization_barrier((odd_inv, residual_t))
    rhs_even = residual_t[0]
    rhs_odd = residual_t[1]

    odd_left = mm("ij,kj->ik", odd_inv, couple_in)
    odd_right = mm("ij,jk->ik", odd_inv, couple_out)
    to_left = mm("ij,jk->ik", couple_in, odd_left)
    to_right = mm("ji,jk->ik", couple_out, odd_right)
    coupling = mm("ij,jk->ik", couple_in, odd_right)
    coupling = jnp.where(position < wall_count - 1, coupling, jnp.zeros_like(coupling))
    rhs_left = mm("ji,jv->iv", odd_left, rhs_odd)
    rhs_right = mm("ji,jv->iv", odd_right, rhs_odd)
    from_left = unpack(
        lax.ppermute(
            jnp.concatenate([to_right, coupling, rhs_right], axis=1),
            "wall",
            pairs_of(range(wall_count), 1, wall_count),
        ),
        unknowns,
    )
    diag = diag_even - to_left - from_left[0]
    upper_right = coupling
    upper_left = from_left[1]
    rhs = rhs_even + rhs_left + from_left[2]

    stride = 1
    while stride < wall_count:
        inv = inverse_spd(diag)
        left = mm("ij,kj->ik", inv, upper_left)
        right = mm("ij,jk->ik", inv, upper_right)
        to_left = mm("ij,jk->ik", upper_left, left)
        to_right = mm("ji,jk->ik", upper_right, right)
        coupling = mm("ij,jk->ik", upper_left, right)
        rhs_left = mm("ji,jv->iv", left, rhs)
        rhs_right = mm("ji,jv->iv", right, rhs)
        from_right = unpack(
            lax.ppermute(
                jnp.concatenate([to_left, coupling, rhs_left], axis=1),
                "wall",
                pairs_of(range(wall_count), -stride, wall_count),
            ),
            unknowns,
        )
        from_left = unpack(
            lax.ppermute(
                jnp.concatenate([to_right, coupling, rhs_right], axis=1),
                "wall",
                pairs_of(range(wall_count), stride, wall_count),
            ),
            unknowns,
        )
        diag = diag - from_right[0] - from_left[0]
        upper_right = from_right[1]
        upper_left = from_left[1]
        rhs = rhs + from_right[2] + from_left[2]
        stride *= 2

    values = mm("ij,jv->iv", inverse_spd(diag), rhs)

    next_values = lax.ppermute(values, "wall", pairs_of(range(1, wall_count), -1, wall_count))
    odd_values = (
        mm("ij,jv->iv", odd_inv, rhs_odd)
        + mm("ij,jv->iv", odd_left, values)
        + mm("ij,jv->iv", odd_right, next_values)
    )
    own = jnp.stack([values, odd_values], axis=0)
    return jnp.swapaxes(own, 1, 2)[None, None]


def solution(mesh):
    placed = (
        P("span", "stream", "wall", None, None),
        P("span", "stream", "wall", None, None),
        P(),
        P(),
        P(),
        P("span", "stream", "wall"),
        P("span", "stream", "wall", None),
        P("span", "stream", "wall", None),
    )
    return jax.shard_map(
        on_device,
        mesh=mesh,
        in_specs=placed,
        out_specs=P("span", "stream", "wall", None, None),
        check_vma=False,
    )
```

```python
import jax
import jax.numpy as jnp
from jax import lax
from jax.experimental import pallas as pl
from jax.experimental.pallas import tpu as pltpu
from jax.sharding import PartitionSpec as P

HIGHEST = lax.Precision.HIGHEST


def shifted(cells, axis, by):
    count = lax.axis_size(axis)
    return lax.ppermute(cells, axis, [(i, (i + by) % count) for i in range(count)])


def mm(spec, a, b):
    return jnp.einsum(spec, a, b, precision=HIGHEST)


PANEL = 128


def panel_inverse(block, scratch):
    size = block.shape[0]
    rows = lax.broadcasted_iota(jnp.int32, (size, size), 0)
    cols = lax.broadcasted_iota(jnp.int32, (size, size), 1)
    row_ids = lax.broadcasted_iota(jnp.int32, (size, 1), 0)
    col_ids = lax.broadcasted_iota(jnp.int32, (1, size), 1)
    scratch[...] = block

    def step(k, carry):
        current = scratch[...]
        row_k = scratch[pl.ds(k, 1), :]
        on_col = cols == k
        col_k = jnp.sum(jnp.where(on_col, current, 0.0), axis=1, keepdims=True)
        pivot = jnp.sum(jnp.where(col_ids == k, row_k, 0.0), axis=1, keepdims=True)
        scaled = jnp.where(col_ids == k, 1.0, row_k) / pivot
        factor = jnp.where(row_ids == k, 0.0, col_k)
        current = jnp.where(on_col, 0.0, current) - factor * scaled
        scratch[...] = jnp.where(rows == k, scaled, current)
        return carry

    lax.fori_loop(0, size, step, 0)
    return scratch[...]


def inverse_kernel(a_ref, o_ref, scratch):
    size = a_ref.shape[0]
    o_ref[...] = a_ref[...]
    row_ids = lax.broadcasted_iota(jnp.int32, (size, PANEL), 0)
    col_ids = lax.broadcasted_iota(jnp.int32, (PANEL, size), 1)
    lane_rows = lax.broadcasted_iota(jnp.int32, (PANEL, size), 0)
    for p in range(size // PANEL):
        part = slice(p * PANEL, (p + 1) * PANEL)
        inv = panel_inverse(o_ref[part, part], scratch)
        rows = o_ref[part, :]
        rows = jnp.where(
            (col_ids >= p * PANEL) & (col_ids < (p + 1) * PANEL),
            (col_ids - p * PANEL == lane_rows).astype(jnp.float32),
            rows,
        )
        new_rows = jnp.dot(inv, rows, precision=HIGHEST, preferred_element_type=jnp.float32)
        col = o_ref[:, part]
        col = jnp.where((row_ids >= p * PANEL) & (row_ids < (p + 1) * PANEL), 0.0, col)
        o_ref[:, part] = jnp.zeros((size, PANEL), jnp.float32)
        o_ref[...] = o_ref[...] - jnp.dot(col, new_rows, precision=HIGHEST, preferred_element_type=jnp.float32)
        o_ref[part, :] = new_rows


def inverse_spd(block):
    size = block.shape[-1]
    padded_size = -(-size // PANEL) * PANEL
    padded = jnp.pad(block, ((0, padded_size - size), (0, padded_size - size)))
    extra = (jnp.arange(padded_size) >= size).astype(block.dtype)
    padded = padded + jnp.diag(extra)
    out = pl.pallas_call(
        inverse_kernel,
        out_shape=jax.ShapeDtypeStruct((padded_size, padded_size), jnp.float32),
        in_specs=[pl.BlockSpec(memory_space=pltpu.VMEM)],
        out_specs=pl.BlockSpec(memory_space=pltpu.VMEM),
        scratch_shapes=[pltpu.VMEM((PANEL, PANEL), jnp.float32)],
    )(padded)
    return out[:size, :size]


def unpack(packed, unknowns):
    return packed[:, :unknowns], packed[:, unknowns : 2 * unknowns], packed[:, 2 * unknowns :]


def unpack2(packed, unknowns):
    return packed[:, :unknowns], packed[:, unknowns:]


def pairs_of(sources, shift, count):
    return [(v, v + shift) for v in sources if 0 <= v + shift < count]


def on_device(
    right_side,
    old_values,
    element_library,
    wall_library,
    face_library,
    element_index,
    wall_faces,
    face_index,
):
    local_side = right_side[0, 0]
    assert local_side.shape[0] == 2
    wall_count = lax.axis_size("wall")
    position = lax.axis_index("wall")
    own_index = element_index[0, 0]
    own_faces = wall_faces[0, 0]
    rates = element_library[own_index]
    below = wall_library[own_faces[:, 0]]
    above = wall_library[own_faces[:, 1]]
    unknowns = rates.shape[1]
    eye = jnp.eye(unknowns, dtype=rates.dtype)
    diag_even = below[0] + above[0] + rates[0][:, None] * eye
    diag_odd = below[1] + above[1] + rates[1][:, None] * eye
    couple_in = below[1]
    couple_out = above[1]

    odd_inv = inverse_spd(diag_odd)

    near_rows = jnp.stack(
        [
            shifted(old_values, "span", 1),
            shifted(old_values, "span", -1),
            shifted(old_values, "stream", 1),
            shifted(old_values, "stream", -1),
        ],
        axis=3,
    )[0, 0]
    blocks = face_library[face_index[0, 0]]
    coupled = mm("edjk,edvk->ejv", blocks, near_rows)
    residual_t = jnp.swapaxes(local_side, 1, 2) - coupled
    odd_inv, residual_t = lax.optimization_barrier((odd_inv, residual_t))
    rhs_even = residual_t[0]
    rhs_odd = residual_t[1]

    odd_left = mm("ij,kj->ik", odd_inv, couple_in)
    odd_right = mm("ij,jk->ik", odd_inv, couple_out)
    to_left = mm("ij,jk->ik", couple_in, odd_left)
    to_right = mm("ji,jk->ik", couple_out, odd_right)
    coupling = mm("ij,jk->ik", couple_in, odd_right)
    coupling = jnp.where(position < wall_count - 1, coupling, jnp.zeros_like(coupling))
    rhs_left = mm("ji,jv->iv", odd_left, rhs_odd)
    rhs_right = mm("ji,jv->iv", odd_right, rhs_odd)
    from_left = unpack(
        lax.ppermute(
            jnp.concatenate([to_right, coupling, rhs_right], axis=1),
            "wall",
            pairs_of(range(wall_count), 1, wall_count),
        ),
        unknowns,
    )
    diag = diag_even - to_left - from_left[0]
    upper_right = coupling
    upper_left = from_left[1]
    rhs = rhs_even + rhs_left + from_left[2]

    stride = 1
    while 2 * stride < wall_count:
        inv = inverse_spd(diag)
        left = mm("ij,kj->ik", inv, upper_left)
        right = mm("ij,jk->ik", inv, upper_right)
        to_left = mm("ij,jk->ik", upper_left, left)
        to_right = mm("ji,jk->ik", upper_right, right)
        coupling = mm("ij,jk->ik", upper_left, right)
        rhs_left = mm("ji,jv->iv", left, rhs)
        rhs_right = mm("ji,jv->iv", right, rhs)
        from_right = unpack(
            lax.ppermute(
                jnp.concatenate([to_left, coupling, rhs_left], axis=1),
                "wall",
                pairs_of(range(wall_count), -stride, wall_count),
            ),
            unknowns,
        )
        from_left = unpack(
            lax.ppermute(
                jnp.concatenate([to_right, coupling, rhs_right], axis=1),
                "wall",
                pairs_of(range(wall_count), stride, wall_count),
            ),
            unknowns,
        )
        diag = diag - from_right[0] - from_left[0]
        upper_right = from_right[1]
        upper_left = from_left[1]
        rhs = rhs + from_right[2] + from_left[2]
        stride *= 2

    if stride < wall_count:
        partner_pairs = [(v, (v + stride) % wall_count) for v in range(wall_count)]
        partner = unpack2(
            lax.ppermute(jnp.concatenate([diag, rhs], axis=1), "wall", partner_pairs), unknowns
        )
        cross = upper_right + jnp.swapaxes(upper_left, 0, 1)
        pair = jnp.concatenate(
            [
                jnp.concatenate([diag, -cross], axis=1),
                jnp.concatenate([-jnp.swapaxes(cross, 0, 1), partner[0]], axis=1),
            ],
            axis=0,
        )
        pair_inv = inverse_spd(pair)
        values = mm("ij,jv->iv", pair_inv[:unknowns, :unknowns], rhs) + mm(
            "ij,jv->iv", pair_inv[:unknowns, unknowns:], partner[1]
        )
    else:
        values = mm("ij,jv->iv", inverse_spd(diag), rhs)

    next_values = lax.ppermute(values, "wall", pairs_of(range(1, wall_count), -1, wall_count))
    odd_values = (
        mm("ij,jv->iv", odd_inv, rhs_odd)
        + mm("ij,jv->iv", odd_left, values)
        + mm("ij,jv->iv", odd_right, next_values)
    )
    own = jnp.stack([values, odd_values], axis=0)
    return jnp.swapaxes(own, 1, 2)[None, None]


def solution(mesh):
    placed = (
        P("span", "stream", "wall", None, None),
        P("span", "stream", "wall", None, None),
        P(),
        P(),
        P(),
        P("span", "stream", "wall"),
        P("span", "stream", "wall", None),
        P("span", "stream", "wall", None),
    )
    return jax.shard_map(
        on_device,
        mesh=mesh,
        in_specs=placed,
        out_specs=P("span", "stream", "wall", None, None),
        check_vma=False,
    )
```

```python
import jax
import jax.numpy as jnp
from jax import lax
from jax.experimental import pallas as pl
from jax.experimental.pallas import tpu as pltpu
from jax.sharding import PartitionSpec as P

HIGHEST = lax.Precision.HIGHEST


def shifted(cells, axis, by):
    count = lax.axis_size(axis)
    return lax.ppermute(cells, axis, [(i, (i + by) % count) for i in range(count)])


def mm(spec, a, b):
    return jnp.einsum(spec, a, b, precision=HIGHEST)


PANEL = 128


def panel_inverse(block, scratch):
    size = block.shape[0]
    rows = lax.broadcasted_iota(jnp.int32, (size, size), 0)
    cols = lax.broadcasted_iota(jnp.int32, (size, size), 1)
    row_ids = lax.broadcasted_iota(jnp.int32, (size, 1), 0)
    col_ids = lax.broadcasted_iota(jnp.int32, (1, size), 1)
    scratch[...] = block

    def pick(row, at):
        return jnp.sum(jnp.where(col_ids == at, row, 0.0), axis=1, keepdims=True)

    def step(j, carry):
        k = 2 * j
        current = scratch[...]
        row_a = scratch[pl.ds(k, 1), :]
        row_b = scratch[pl.ds(k + 1, 1), :]
        col_a = jnp.sum(jnp.where(cols == k, current, 0.0), axis=1, keepdims=True)
        col_b = jnp.sum(jnp.where(cols == k + 1, current, 0.0), axis=1, keepdims=True)
        p00 = pick(row_a, k)
        p01 = pick(row_a, k + 1)
        p10 = pick(row_b, k)
        p11 = pick(row_b, k + 1)
        det = p00 * p11 - p01 * p10
        row_a = jnp.where(col_ids == k, 1.0, jnp.where(col_ids == k + 1, 0.0, row_a))
        row_b = jnp.where(col_ids == k, 0.0, jnp.where(col_ids == k + 1, 1.0, row_b))
        new_a = (p11 * row_a - p01 * row_b) / det
        new_b = (p00 * row_b - p10 * row_a) / det
        in_pair = (row_ids == k) | (row_ids == k + 1)
        col_a = jnp.where(in_pair, 0.0, col_a)
        col_b = jnp.where(in_pair, 0.0, col_b)
        on_cols = (cols == k) | (cols == k + 1)
        current = jnp.where(on_cols, 0.0, current) - col_a * new_a - col_b * new_b
        current = jnp.where(rows == k, new_a, jnp.where(rows == k + 1, new_b, current))
        scratch[...] = current
        return carry

    lax.fori_loop(0, size // 2, step, 0)
    return scratch[...]


def inverse_kernel(a_ref, o_ref, scratch):
    size = a_ref.shape[0]
    o_ref[...] = a_ref[...]
    row_ids = lax.broadcasted_iota(jnp.int32, (size, PANEL), 0)
    col_ids = lax.broadcasted_iota(jnp.int32, (PANEL, size), 1)
    lane_rows = lax.broadcasted_iota(jnp.int32, (PANEL, size), 0)
    for p in range(size // PANEL):
        part = slice(p * PANEL, (p + 1) * PANEL)
        inv = panel_inverse(o_ref[part, part], scratch)
        rows = o_ref[part, :]
        rows = jnp.where(
            (col_ids >= p * PANEL) & (col_ids < (p + 1) * PANEL),
            (col_ids - p * PANEL == lane_rows).astype(jnp.float32),
            rows,
        )
        new_rows = jnp.dot(inv, rows, precision=HIGHEST, preferred_element_type=jnp.float32)
        col = o_ref[:, part]
        col = jnp.where((row_ids >= p * PANEL) & (row_ids < (p + 1) * PANEL), 0.0, col)
        o_ref[:, part] = jnp.zeros((size, PANEL), jnp.float32)
        o_ref[...] = o_ref[...] - jnp.dot(col, new_rows, precision=HIGHEST, preferred_element_type=jnp.float32)
        o_ref[part, :] = new_rows


def inverse_spd(block):
    size = block.shape[-1]
    padded_size = -(-size // PANEL) * PANEL
    padded = jnp.pad(block, ((0, padded_size - size), (0, padded_size - size)))
    extra = (jnp.arange(padded_size) >= size).astype(block.dtype)
    padded = padded + jnp.diag(extra)
    out = pl.pallas_call(
        inverse_kernel,
        out_shape=jax.ShapeDtypeStruct((padded_size, padded_size), jnp.float32),
        in_specs=[pl.BlockSpec(memory_space=pltpu.VMEM)],
        out_specs=pl.BlockSpec(memory_space=pltpu.VMEM),
        scratch_shapes=[pltpu.VMEM((PANEL, PANEL), jnp.float32)],
    )(padded)
    return out[:size, :size]


def unpack(packed, unknowns):
    return packed[:, :unknowns], packed[:, unknowns : 2 * unknowns], packed[:, 2 * unknowns :]


def unpack2(packed, unknowns):
    return packed[:, :unknowns], packed[:, unknowns:]


def pairs_of(sources, shift, count):
    return [(v, v + shift) for v in sources if 0 <= v + shift < count]


def on_device(
    right_side,
    old_values,
    element_library,
    wall_library,
    face_library,
    element_index,
    wall_faces,
    face_index,
):
    local_side = right_side[0, 0]
    assert local_side.shape[0] == 2
    wall_count = lax.axis_size("wall")
    position = lax.axis_index("wall")
    own_index = element_index[0, 0]
    own_faces = wall_faces[0, 0]
    rates = element_library[own_index]
    below = wall_library[own_faces[:, 0]]
    above = wall_library[own_faces[:, 1]]
    unknowns = rates.shape[1]
    eye = jnp.eye(unknowns, dtype=rates.dtype)
    diag_even = below[0] + above[0] + rates[0][:, None] * eye
    diag_odd = below[1] + above[1] + rates[1][:, None] * eye
    couple_in = below[1]
    couple_out = above[1]

    odd_inv = inverse_spd(diag_odd)

    near_rows = jnp.stack(
        [
            shifted(old_values, "span", 1),
            shifted(old_values, "span", -1),
            shifted(old_values, "stream", 1),
            shifted(old_values, "stream", -1),
        ],
        axis=3,
    )[0, 0]
    blocks = face_library[face_index[0, 0]]
    coupled = mm("edjk,edvk->ejv", blocks, near_rows)
    residual_t = jnp.swapaxes(local_side, 1, 2) - coupled
    odd_inv, residual_t = lax.optimization_barrier((odd_inv, residual_t))
    rhs_even = residual_t[0]
    rhs_odd = residual_t[1]

    odd_left = mm("ij,kj->ik", odd_inv, couple_in)
    odd_right = mm("ij,jk->ik", odd_inv, couple_out)
    to_left = mm("ij,jk->ik", couple_in, odd_left)
    to_right = mm("ji,jk->ik", couple_out, odd_right)
    coupling = mm("ij,jk->ik", couple_in, odd_right)
    coupling = jnp.where(position < wall_count - 1, coupling, jnp.zeros_like(coupling))
    rhs_left = mm("ji,jv->iv", odd_left, rhs_odd)
    rhs_right = mm("ji,jv->iv", odd_right, rhs_odd)
    from_left = unpack(
        lax.ppermute(
            jnp.concatenate([to_right, coupling, rhs_right], axis=1),
            "wall",
            pairs_of(range(wall_count), 1, wall_count),
        ),
        unknowns,
    )
    diag = diag_even - to_left - from_left[0]
    upper_right = coupling
    upper_left = from_left[1]
    rhs = rhs_even + rhs_left + from_left[2]

    stride = 1
    while 2 * stride < wall_count:
        inv = inverse_spd(diag)
        left = mm("ij,kj->ik", inv, upper_left)
        right = mm("ij,jk->ik", inv, upper_right)
        to_left = mm("ij,jk->ik", upper_left, left)
        to_right = mm("ji,jk->ik", upper_right, right)
        coupling = mm("ij,jk->ik", upper_left, right)
        rhs_left = mm("ji,jv->iv", left, rhs)
        rhs_right = mm("ji,jv->iv", right, rhs)
        from_right = unpack(
            lax.ppermute(
                jnp.concatenate([to_left, coupling, rhs_left], axis=1),
                "wall",
                pairs_of(range(wall_count), -stride, wall_count),
            ),
            unknowns,
        )
        from_left = unpack(
            lax.ppermute(
                jnp.concatenate([to_right, coupling, rhs_right], axis=1),
                "wall",
                pairs_of(range(wall_count), stride, wall_count),
            ),
            unknowns,
        )
        diag = diag - from_right[0] - from_left[0]
        upper_right = from_right[1]
        upper_left = from_left[1]
        rhs = rhs + from_right[2] + from_left[2]
        stride *= 2

    if stride < wall_count:
        partner_pairs = [(v, (v + stride) % wall_count) for v in range(wall_count)]
        partner = unpack2(
            lax.ppermute(jnp.concatenate([diag, rhs], axis=1), "wall", partner_pairs), unknowns
        )
        cross = upper_right + jnp.swapaxes(upper_left, 0, 1)
        pair = jnp.concatenate(
            [
                jnp.concatenate([diag, -cross], axis=1),
                jnp.concatenate([-jnp.swapaxes(cross, 0, 1), partner[0]], axis=1),
            ],
            axis=0,
        )
        pair_inv = inverse_spd(pair)
        values = mm("ij,jv->iv", pair_inv[:unknowns, :unknowns], rhs) + mm(
            "ij,jv->iv", pair_inv[:unknowns, unknowns:], partner[1]
        )
    else:
        values = mm("ij,jv->iv", inverse_spd(diag), rhs)

    next_values = lax.ppermute(values, "wall", pairs_of(range(1, wall_count), -1, wall_count))
    odd_values = (
        mm("ij,jv->iv", odd_inv, rhs_odd)
        + mm("ij,jv->iv", odd_left, values)
        + mm("ij,jv->iv", odd_right, next_values)
    )
    own = jnp.stack([values, odd_values], axis=0)
    return jnp.swapaxes(own, 1, 2)[None, None]


def solution(mesh):
    placed = (
        P("span", "stream", "wall", None, None),
        P("span", "stream", "wall", None, None),
        P(),
        P(),
        P(),
        P("span", "stream", "wall"),
        P("span", "stream", "wall", None),
        P("span", "stream", "wall", None),
    )
    return jax.shard_map(
        on_device,
        mesh=mesh,
        in_specs=placed,
        out_specs=P("span", "stream", "wall", None, None),
        check_vma=False,
    )
```

```python
import jax
import jax.numpy as jnp
from jax import lax
from jax.experimental import pallas as pl
from jax.experimental.pallas import tpu as pltpu
from jax.sharding import PartitionSpec as P

HIGHEST = lax.Precision.HIGHEST


def shifted(cells, axis, by):
    count = lax.axis_size(axis)
    return lax.ppermute(cells, axis, [(i, (i + by) % count) for i in range(count)])


def mm(spec, a, b):
    return jnp.einsum(spec, a, b, precision=HIGHEST)


PANEL = 128


GROUP = 4


def small_inverse(entries):
    count = len(entries)
    work = [list(row) + [1.0 if i == j else 0.0 for j in range(count)] for i, row in enumerate(entries)]
    for t in range(count):
        scale = 1.0 / work[t][t]
        work[t] = [value * scale for value in work[t]]
        for i in range(count):
            if i != t:
                factor = work[i][t]
                work[i] = [a - factor * b for a, b in zip(work[i], work[t])]
    return [row[count:] for row in work]


def panel_inverse(block, scratch):
    size = block.shape[0]
    rows = lax.broadcasted_iota(jnp.int32, (size, size), 0)
    cols = lax.broadcasted_iota(jnp.int32, (size, size), 1)
    row_ids = lax.broadcasted_iota(jnp.int32, (size, 1), 0)
    col_ids = lax.broadcasted_iota(jnp.int32, (1, size), 1)
    scratch[...] = block

    def step(j, carry):
        k = GROUP * j
        current = scratch[...]
        picked = [scratch[pl.ds(k + t, 1), :] for t in range(GROUP)]
        columns = [
            jnp.sum(jnp.where(cols == k + t, current, 0.0), axis=1, keepdims=True) for t in range(GROUP)
        ]
        entries = [
            [jnp.sum(jnp.where(col_ids == k + u, picked[t], 0.0), axis=1, keepdims=True) for u in range(GROUP)]
            for t in range(GROUP)
        ]
        inverse = small_inverse(entries)
        unit = [(col_ids == k + t).astype(jnp.float32) for t in range(GROUP)]
        in_group = (col_ids >= k) & (col_ids < k + GROUP)
        picked = [jnp.where(in_group, unit[t], picked[t]) for t in range(GROUP)]
        fresh = []
        for t in range(GROUP):
            total = inverse[t][0] * picked[0]
            for u in range(1, GROUP):
                total = total + inverse[t][u] * picked[u]
            fresh.append(total)
        in_rows = (row_ids >= k) & (row_ids < k + GROUP)
        on_cols = (cols >= k) & (cols < k + GROUP)
        current = jnp.where(on_cols, 0.0, current)
        for t in range(GROUP):
            current = current - jnp.where(in_rows, 0.0, columns[t]) * fresh[t]
        for t in range(GROUP):
            current = jnp.where(rows == k + t, fresh[t], current)
        scratch[...] = current
        return carry

    lax.fori_loop(0, size // GROUP, step, 0)
    return scratch[...]


def inverse_kernel(a_ref, o_ref, scratch):
    size = a_ref.shape[0]
    o_ref[...] = a_ref[...]
    row_ids = lax.broadcasted_iota(jnp.int32, (size, PANEL), 0)
    col_ids = lax.broadcasted_iota(jnp.int32, (PANEL, size), 1)
    lane_rows = lax.broadcasted_iota(jnp.int32, (PANEL, size), 0)
    for p in range(size // PANEL):
        part = slice(p * PANEL, (p + 1) * PANEL)
        inv = panel_inverse(o_ref[part, part], scratch)
        rows = o_ref[part, :]
        rows = jnp.where(
            (col_ids >= p * PANEL) & (col_ids < (p + 1) * PANEL),
            (col_ids - p * PANEL == lane_rows).astype(jnp.float32),
            rows,
        )
        new_rows = jnp.dot(inv, rows, precision=HIGHEST, preferred_element_type=jnp.float32)
        col = o_ref[:, part]
        col = jnp.where((row_ids >= p * PANEL) & (row_ids < (p + 1) * PANEL), 0.0, col)
        o_ref[:, part] = jnp.zeros((size, PANEL), jnp.float32)
        o_ref[...] = o_ref[...] - jnp.dot(col, new_rows, precision=HIGHEST, preferred_element_type=jnp.float32)
        o_ref[part, :] = new_rows


def inverse_spd(block):
    size = block.shape[-1]
    padded_size = -(-size // PANEL) * PANEL
    padded = jnp.pad(block, ((0, padded_size - size), (0, padded_size - size)))
    extra = (jnp.arange(padded_size) >= size).astype(block.dtype)
    padded = padded + jnp.diag(extra)
    out = pl.pallas_call(
        inverse_kernel,
        out_shape=jax.ShapeDtypeStruct((padded_size, padded_size), jnp.float32),
        in_specs=[pl.BlockSpec(memory_space=pltpu.VMEM)],
        out_specs=pl.BlockSpec(memory_space=pltpu.VMEM),
        scratch_shapes=[pltpu.VMEM((PANEL, PANEL), jnp.float32)],
    )(padded)
    return out[:size, :size]


def unpack(packed, unknowns):
    return packed[:, :unknowns], packed[:, unknowns : 2 * unknowns], packed[:, 2 * unknowns :]


def unpack2(packed, unknowns):
    return packed[:, :unknowns], packed[:, unknowns:]


def pairs_of(sources, shift, count):
    return [(v, v + shift) for v in sources if 0 <= v + shift < count]


def on_device(
    right_side,
    old_values,
    element_library,
    wall_library,
    face_library,
    element_index,
    wall_faces,
    face_index,
):
    local_side = right_side[0, 0]
    assert local_side.shape[0] == 2
    wall_count = lax.axis_size("wall")
    position = lax.axis_index("wall")
    own_index = element_index[0, 0]
    own_faces = wall_faces[0, 0]
    rates = element_library[own_index]
    below = wall_library[own_faces[:, 0]]
    above = wall_library[own_faces[:, 1]]
    unknowns = rates.shape[1]
    eye = jnp.eye(unknowns, dtype=rates.dtype)
    diag_even = below[0] + above[0] + rates[0][:, None] * eye
    diag_odd = below[1] + above[1] + rates[1][:, None] * eye
    couple_in = below[1]
    couple_out = above[1]

    odd_inv = inverse_spd(diag_odd)

    near_rows = jnp.stack(
        [
            shifted(old_values, "span", 1),
            shifted(old_values, "span", -1),
            shifted(old_values, "stream", 1),
            shifted(old_values, "stream", -1),
        ],
        axis=3,
    )[0, 0]
    blocks = face_library[face_index[0, 0]]
    coupled = mm("edjk,edvk->ejv", blocks, near_rows)
    residual_t = jnp.swapaxes(local_side, 1, 2) - coupled
    odd_inv, residual_t = lax.optimization_barrier((odd_inv, residual_t))
    rhs_even = residual_t[0]
    rhs_odd = residual_t[1]

    odd_left = mm("ij,kj->ik", odd_inv, couple_in)
    odd_right = mm("ij,jk->ik", odd_inv, couple_out)
    to_left = mm("ij,jk->ik", couple_in, odd_left)
    to_right = mm("ji,jk->ik", couple_out, odd_right)
    coupling = mm("ij,jk->ik", couple_in, odd_right)
    coupling = jnp.where(position < wall_count - 1, coupling, jnp.zeros_like(coupling))
    rhs_left = mm("ji,jv->iv", odd_left, rhs_odd)
    rhs_right = mm("ji,jv->iv", odd_right, rhs_odd)
    from_left = unpack(
        lax.ppermute(
            jnp.concatenate([to_right, coupling, rhs_right], axis=1),
            "wall",
            pairs_of(range(wall_count), 1, wall_count),
        ),
        unknowns,
    )
    diag = diag_even - to_left - from_left[0]
    upper_right = coupling
    upper_left = from_left[1]
    rhs = rhs_even + rhs_left + from_left[2]

    stride = 1
    while 2 * stride < wall_count:
        inv = inverse_spd(diag)
        left = mm("ij,kj->ik", inv, upper_left)
        right = mm("ij,jk->ik", inv, upper_right)
        to_left = mm("ij,jk->ik", upper_left, left)
        to_right = mm("ji,jk->ik", upper_right, right)
        coupling = mm("ij,jk->ik", upper_left, right)
        rhs_left = mm("ji,jv->iv", left, rhs)
        rhs_right = mm("ji,jv->iv", right, rhs)
        from_right = unpack(
            lax.ppermute(
                jnp.concatenate([to_left, coupling, rhs_left], axis=1),
                "wall",
                pairs_of(range(wall_count), -stride, wall_count),
            ),
            unknowns,
        )
        from_left = unpack(
            lax.ppermute(
                jnp.concatenate([to_right, coupling, rhs_right], axis=1),
                "wall",
                pairs_of(range(wall_count), stride, wall_count),
            ),
            unknowns,
        )
        diag = diag - from_right[0] - from_left[0]
        upper_right = from_right[1]
        upper_left = from_left[1]
        rhs = rhs + from_right[2] + from_left[2]
        stride *= 2

    if stride < wall_count:
        partner_pairs = [(v, (v + stride) % wall_count) for v in range(wall_count)]
        partner = unpack2(
            lax.ppermute(jnp.concatenate([diag, rhs], axis=1), "wall", partner_pairs), unknowns
        )
        cross = upper_right + jnp.swapaxes(upper_left, 0, 1)
        pair = jnp.concatenate(
            [
                jnp.concatenate([diag, -cross], axis=1),
                jnp.concatenate([-jnp.swapaxes(cross, 0, 1), partner[0]], axis=1),
            ],
            axis=0,
        )
        pair_inv = inverse_spd(pair)
        values = mm("ij,jv->iv", pair_inv[:unknowns, :unknowns], rhs) + mm(
            "ij,jv->iv", pair_inv[:unknowns, unknowns:], partner[1]
        )
    else:
        values = mm("ij,jv->iv", inverse_spd(diag), rhs)

    next_values = lax.ppermute(values, "wall", pairs_of(range(1, wall_count), -1, wall_count))
    odd_values = (
        mm("ij,jv->iv", odd_inv, rhs_odd)
        + mm("ij,jv->iv", odd_left, values)
        + mm("ij,jv->iv", odd_right, next_values)
    )
    own = jnp.stack([values, odd_values], axis=0)
    return jnp.swapaxes(own, 1, 2)[None, None]


def solution(mesh):
    placed = (
        P("span", "stream", "wall", None, None),
        P("span", "stream", "wall", None, None),
        P(),
        P(),
        P(),
        P("span", "stream", "wall"),
        P("span", "stream", "wall", None),
        P("span", "stream", "wall", None),
    )
    return jax.shard_map(
        on_device,
        mesh=mesh,
        in_specs=placed,
        out_specs=P("span", "stream", "wall", None, None),
        check_vma=False,
    )
```

```python
import jax
import jax.numpy as jnp
from jax import lax
from jax.experimental import pallas as pl
from jax.experimental.pallas import tpu as pltpu
from jax.sharding import PartitionSpec as P

HIGHEST = lax.Precision.HIGHEST


def shifted(cells, axis, by):
    count = lax.axis_size(axis)
    return lax.ppermute(cells, axis, [(i, (i + by) % count) for i in range(count)])


def mm(spec, a, b):
    return jnp.einsum(spec, a, b, precision=lax.Precision.HIGH)


PANEL = 128


GROUP = 4


def small_inverse(entries):
    count = len(entries)
    work = [list(row) + [1.0 if i == j else 0.0 for j in range(count)] for i, row in enumerate(entries)]
    for t in range(count):
        scale = 1.0 / work[t][t]
        work[t] = [value * scale for value in work[t]]
        for i in range(count):
            if i != t:
                factor = work[i][t]
                work[i] = [a - factor * b for a, b in zip(work[i], work[t])]
    return [row[count:] for row in work]


def panel_inverse(block, scratch):
    size = block.shape[0]
    rows = lax.broadcasted_iota(jnp.int32, (size, size), 0)
    cols = lax.broadcasted_iota(jnp.int32, (size, size), 1)
    row_ids = lax.broadcasted_iota(jnp.int32, (size, 1), 0)
    col_ids = lax.broadcasted_iota(jnp.int32, (1, size), 1)
    scratch[...] = block

    def step(j, carry):
        k = GROUP * j
        current = scratch[...]
        picked = [scratch[pl.ds(k + t, 1), :] for t in range(GROUP)]
        columns = [
            jnp.sum(jnp.where(cols == k + t, current, 0.0), axis=1, keepdims=True) for t in range(GROUP)
        ]
        entries = [
            [jnp.sum(jnp.where(col_ids == k + u, picked[t], 0.0), axis=1, keepdims=True) for u in range(GROUP)]
            for t in range(GROUP)
        ]
        inverse = small_inverse(entries)
        unit = [(col_ids == k + t).astype(jnp.float32) for t in range(GROUP)]
        in_group = (col_ids >= k) & (col_ids < k + GROUP)
        picked = [jnp.where(in_group, unit[t], picked[t]) for t in range(GROUP)]
        fresh = []
        for t in range(GROUP):
            total = inverse[t][0] * picked[0]
            for u in range(1, GROUP):
                total = total + inverse[t][u] * picked[u]
            fresh.append(total)
        in_rows = (row_ids >= k) & (row_ids < k + GROUP)
        on_cols = (cols >= k) & (cols < k + GROUP)
        current = jnp.where(on_cols, 0.0, current)
        for t in range(GROUP):
            current = current - jnp.where(in_rows, 0.0, columns[t]) * fresh[t]
        for t in range(GROUP):
            current = jnp.where(rows == k + t, fresh[t], current)
        scratch[...] = current
        return carry

    lax.fori_loop(0, size // GROUP, step, 0)
    return scratch[...]


def inverse_kernel(a_ref, o_ref, scratch):
    size = a_ref.shape[0]
    o_ref[...] = a_ref[...]
    row_ids = lax.broadcasted_iota(jnp.int32, (size, PANEL), 0)
    col_ids = lax.broadcasted_iota(jnp.int32, (PANEL, size), 1)
    lane_rows = lax.broadcasted_iota(jnp.int32, (PANEL, size), 0)
    for p in range(size // PANEL):
        part = slice(p * PANEL, (p + 1) * PANEL)
        inv = panel_inverse(o_ref[part, part], scratch)
        rows = o_ref[part, :]
        rows = jnp.where(
            (col_ids >= p * PANEL) & (col_ids < (p + 1) * PANEL),
            (col_ids - p * PANEL == lane_rows).astype(jnp.float32),
            rows,
        )
        new_rows = jnp.dot(inv, rows, precision=HIGHEST, preferred_element_type=jnp.float32)
        col = o_ref[:, part]
        col = jnp.where((row_ids >= p * PANEL) & (row_ids < (p + 1) * PANEL), 0.0, col)
        o_ref[:, part] = jnp.zeros((size, PANEL), jnp.float32)
        o_ref[...] = o_ref[...] - jnp.dot(col, new_rows, precision=HIGHEST, preferred_element_type=jnp.float32)
        o_ref[part, :] = new_rows


def inverse_spd(block):
    size = block.shape[-1]
    padded_size = -(-size // PANEL) * PANEL
    padded = jnp.pad(block, ((0, padded_size - size), (0, padded_size - size)))
    extra = (jnp.arange(padded_size) >= size).astype(block.dtype)
    padded = padded + jnp.diag(extra)
    out = pl.pallas_call(
        inverse_kernel,
        out_shape=jax.ShapeDtypeStruct((padded_size, padded_size), jnp.float32),
        in_specs=[pl.BlockSpec(memory_space=pltpu.VMEM)],
        out_specs=pl.BlockSpec(memory_space=pltpu.VMEM),
        scratch_shapes=[pltpu.VMEM((PANEL, PANEL), jnp.float32)],
    )(padded)
    return out[:size, :size]


def unpack(packed, unknowns):
    return packed[:, :unknowns], packed[:, unknowns : 2 * unknowns], packed[:, 2 * unknowns :]


def unpack2(packed, unknowns):
    return packed[:, :unknowns], packed[:, unknowns:]


def pairs_of(sources, shift, count):
    return [(v, v + shift) for v in sources if 0 <= v + shift < count]


def on_device(
    right_side,
    old_values,
    element_library,
    wall_library,
    face_library,
    element_index,
    wall_faces,
    face_index,
):
    local_side = right_side[0, 0]
    assert local_side.shape[0] == 2
    wall_count = lax.axis_size("wall")
    position = lax.axis_index("wall")
    own_index = element_index[0, 0]
    own_faces = wall_faces[0, 0]
    rates = element_library[own_index]
    below = wall_library[own_faces[:, 0]]
    above = wall_library[own_faces[:, 1]]
    unknowns = rates.shape[1]
    eye = jnp.eye(unknowns, dtype=rates.dtype)
    diag_even = below[0] + above[0] + rates[0][:, None] * eye
    diag_odd = below[1] + above[1] + rates[1][:, None] * eye
    couple_in = below[1]
    couple_out = above[1]

    odd_inv = inverse_spd(diag_odd)

    near_rows = jnp.stack(
        [
            shifted(old_values, "span", 1),
            shifted(old_values, "span", -1),
            shifted(old_values, "stream", 1),
            shifted(old_values, "stream", -1),
        ],
        axis=3,
    )[0, 0]
    blocks = face_library[face_index[0, 0]]
    coupled = mm("edjk,edvk->ejv", blocks, near_rows)
    residual_t = jnp.swapaxes(local_side, 1, 2) - coupled
    odd_inv, residual_t = lax.optimization_barrier((odd_inv, residual_t))
    rhs_even = residual_t[0]
    rhs_odd = residual_t[1]

    odd_left = mm("ij,kj->ik", odd_inv, couple_in)
    odd_right = mm("ij,jk->ik", odd_inv, couple_out)
    to_left = mm("ij,jk->ik", couple_in, odd_left)
    to_right = mm("ji,jk->ik", couple_out, odd_right)
    coupling = mm("ij,jk->ik", couple_in, odd_right)
    coupling = jnp.where(position < wall_count - 1, coupling, jnp.zeros_like(coupling))
    rhs_left = mm("ji,jv->iv", odd_left, rhs_odd)
    rhs_right = mm("ji,jv->iv", odd_right, rhs_odd)
    from_left = unpack(
        lax.ppermute(
            jnp.concatenate([to_right, coupling, rhs_right], axis=1),
            "wall",
            pairs_of(range(wall_count), 1, wall_count),
        ),
        unknowns,
    )
    diag = diag_even - to_left - from_left[0]
    upper_right = coupling
    upper_left = from_left[1]
    rhs = rhs_even + rhs_left + from_left[2]

    stride = 1
    while 2 * stride < wall_count:
        inv = inverse_spd(diag)
        left = mm("ij,kj->ik", inv, upper_left)
        right = mm("ij,jk->ik", inv, upper_right)
        to_left = mm("ij,jk->ik", upper_left, left)
        to_right = mm("ji,jk->ik", upper_right, right)
        coupling = mm("ij,jk->ik", upper_left, right)
        rhs_left = mm("ji,jv->iv", left, rhs)
        rhs_right = mm("ji,jv->iv", right, rhs)
        from_right = unpack(
            lax.ppermute(
                jnp.concatenate([to_left, coupling, rhs_left], axis=1),
                "wall",
                pairs_of(range(wall_count), -stride, wall_count),
            ),
            unknowns,
        )
        from_left = unpack(
            lax.ppermute(
                jnp.concatenate([to_right, coupling, rhs_right], axis=1),
                "wall",
                pairs_of(range(wall_count), stride, wall_count),
            ),
            unknowns,
        )
        diag = diag - from_right[0] - from_left[0]
        upper_right = from_right[1]
        upper_left = from_left[1]
        rhs = rhs + from_right[2] + from_left[2]
        stride *= 2

    if stride < wall_count:
        partner_pairs = [(v, (v + stride) % wall_count) for v in range(wall_count)]
        partner = unpack2(
            lax.ppermute(jnp.concatenate([diag, rhs], axis=1), "wall", partner_pairs), unknowns
        )
        cross = upper_right + jnp.swapaxes(upper_left, 0, 1)
        pair = jnp.concatenate(
            [
                jnp.concatenate([diag, -cross], axis=1),
                jnp.concatenate([-jnp.swapaxes(cross, 0, 1), partner[0]], axis=1),
            ],
            axis=0,
        )
        pair_inv = inverse_spd(pair)
        values = mm("ij,jv->iv", pair_inv[:unknowns, :unknowns], rhs) + mm(
            "ij,jv->iv", pair_inv[:unknowns, unknowns:], partner[1]
        )
    else:
        values = mm("ij,jv->iv", inverse_spd(diag), rhs)

    next_values = lax.ppermute(values, "wall", pairs_of(range(1, wall_count), -1, wall_count))
    odd_values = (
        mm("ij,jv->iv", odd_inv, rhs_odd)
        + mm("ij,jv->iv", odd_left, values)
        + mm("ij,jv->iv", odd_right, next_values)
    )
    own = jnp.stack([values, odd_values], axis=0)
    return jnp.swapaxes(own, 1, 2)[None, None]


def solution(mesh):
    placed = (
        P("span", "stream", "wall", None, None),
        P("span", "stream", "wall", None, None),
        P(),
        P(),
        P(),
        P("span", "stream", "wall"),
        P("span", "stream", "wall", None),
        P("span", "stream", "wall", None),
    )
    return jax.shard_map(
        on_device,
        mesh=mesh,
        in_specs=placed,
        out_specs=P("span", "stream", "wall", None, None),
        check_vma=False,
    )
```

```python
import jax
import jax.numpy as jnp
from jax import lax
from jax.experimental import pallas as pl
from jax.experimental.pallas import tpu as pltpu
from jax.sharding import PartitionSpec as P

HIGHEST = lax.Precision.HIGHEST


def shifted(cells, axis, by):
    count = lax.axis_size(axis)
    return lax.ppermute(cells, axis, [(i, (i + by) % count) for i in range(count)])


def mm(spec, a, b):
    return jnp.einsum(spec, a, b, precision=HIGHEST)


PANEL = 128


GROUP = 4


def small_inverse(entries):
    count = len(entries)
    work = [list(row) + [1.0 if i == j else 0.0 for j in range(count)] for i, row in enumerate(entries)]
    for t in range(count):
        scale = 1.0 / work[t][t]
        work[t] = [value * scale for value in work[t]]
        for i in range(count):
            if i != t:
                factor = work[i][t]
                work[i] = [a - factor * b for a, b in zip(work[i], work[t])]
    return [row[count:] for row in work]


def panel_inverse(block, scratch):
    size = block.shape[0]
    rows = lax.broadcasted_iota(jnp.int32, (size, size), 0)
    cols = lax.broadcasted_iota(jnp.int32, (size, size), 1)
    row_ids = lax.broadcasted_iota(jnp.int32, (size, 1), 0)
    col_ids = lax.broadcasted_iota(jnp.int32, (1, size), 1)
    scratch[...] = block

    def step(j, carry):
        k = GROUP * j
        current = scratch[...]
        picked = [scratch[pl.ds(k + t, 1), :] for t in range(GROUP)]
        columns = [
            jnp.sum(jnp.where(cols == k + t, current, 0.0), axis=1, keepdims=True) for t in range(GROUP)
        ]
        entries = [
            [jnp.sum(jnp.where(col_ids == k + u, picked[t], 0.0), axis=1, keepdims=True) for u in range(GROUP)]
            for t in range(GROUP)
        ]
        inverse = small_inverse(entries)
        unit = [(col_ids == k + t).astype(jnp.float32) for t in range(GROUP)]
        in_group = (col_ids >= k) & (col_ids < k + GROUP)
        picked = [jnp.where(in_group, unit[t], picked[t]) for t in range(GROUP)]
        fresh = []
        for t in range(GROUP):
            total = inverse[t][0] * picked[0]
            for u in range(1, GROUP):
                total = total + inverse[t][u] * picked[u]
            fresh.append(total)
        in_rows = (row_ids >= k) & (row_ids < k + GROUP)
        on_cols = (cols >= k) & (cols < k + GROUP)
        current = jnp.where(on_cols, 0.0, current)
        for t in range(GROUP):
            current = current - jnp.where(in_rows, 0.0, columns[t]) * fresh[t]
        for t in range(GROUP):
            current = jnp.where(rows == k + t, fresh[t], current)
        scratch[...] = current
        return carry

    lax.fori_loop(0, size // GROUP, step, 0)
    return scratch[...]


def inverse_kernel(a_ref, o_ref, scratch):
    size = a_ref.shape[0]
    o_ref[...] = a_ref[...]
    row_ids = lax.broadcasted_iota(jnp.int32, (size, PANEL), 0)
    col_ids = lax.broadcasted_iota(jnp.int32, (PANEL, size), 1)
    lane_rows = lax.broadcasted_iota(jnp.int32, (PANEL, size), 0)
    for p in range(size // PANEL):
        part = slice(p * PANEL, (p + 1) * PANEL)
        inv = panel_inverse(o_ref[part, part], scratch)
        rows = o_ref[part, :]
        rows = jnp.where(
            (col_ids >= p * PANEL) & (col_ids < (p + 1) * PANEL),
            (col_ids - p * PANEL == lane_rows).astype(jnp.float32),
            rows,
        )
        new_rows = jnp.dot(inv, rows, precision=HIGHEST, preferred_element_type=jnp.float32)
        col = o_ref[:, part]
        col = jnp.where((row_ids >= p * PANEL) & (row_ids < (p + 1) * PANEL), 0.0, col)
        o_ref[:, part] = jnp.zeros((size, PANEL), jnp.float32)
        o_ref[...] = o_ref[...] - jnp.dot(col, new_rows, precision=HIGHEST, preferred_element_type=jnp.float32)
        o_ref[part, :] = new_rows


def inverse_spd(block):
    size = block.shape[-1]
    padded_size = -(-size // PANEL) * PANEL
    padded = jnp.pad(block, ((0, padded_size - size), (0, padded_size - size)))
    extra = (jnp.arange(padded_size) >= size).astype(block.dtype)
    padded = padded + jnp.diag(extra)
    out = pl.pallas_call(
        inverse_kernel,
        out_shape=jax.ShapeDtypeStruct((padded_size, padded_size), jnp.float32),
        in_specs=[pl.BlockSpec(memory_space=pltpu.VMEM)],
        out_specs=pl.BlockSpec(memory_space=pltpu.VMEM),
        scratch_shapes=[pltpu.VMEM((PANEL, PANEL), jnp.float32)],
    )(padded)
    return out[:size, :size]


def unpack(packed, unknowns):
    return packed[:, :unknowns], packed[:, unknowns : 2 * unknowns], packed[:, 2 * unknowns :]


def unpack2(packed, unknowns):
    return packed[:, :unknowns], packed[:, unknowns:]


def pairs_of(sources, shift, count):
    return [(v, v + shift) for v in sources if 0 <= v + shift < count]


def on_device(
    right_side,
    old_values,
    element_library,
    wall_library,
    face_library,
    element_index,
    wall_faces,
    face_index,
):
    local_side = right_side[0, 0]
    assert local_side.shape[0] == 2
    wall_count = lax.axis_size("wall")
    position = lax.axis_index("wall")
    own_index = element_index[0, 0]
    own_faces = wall_faces[0, 0]
    rates = element_library[own_index]
    below = wall_library[own_faces[:, 0]]
    above = wall_library[own_faces[:, 1]]
    unknowns = rates.shape[1]
    eye = jnp.eye(unknowns, dtype=rates.dtype)
    diag_even = below[0] + above[0] + rates[0][:, None] * eye
    diag_odd = below[1] + above[1] + rates[1][:, None] * eye
    couple_in = below[1]
    couple_out = above[1]

    odd_inv = inverse_spd(diag_odd)

    near_rows = jnp.stack(
        [
            shifted(old_values, "span", 1),
            shifted(old_values, "span", -1),
            shifted(old_values, "stream", 1),
            shifted(old_values, "stream", -1),
        ],
        axis=3,
    )[0, 0]
    blocks = face_library[face_index[0, 0]]
    coupled = mm("edjk,edvk->ejv", blocks, near_rows)
    residual_t = jnp.swapaxes(local_side, 1, 2) - coupled

    rhs_even = residual_t[0]
    rhs_odd = residual_t[1]

    odd_left = mm("ij,kj->ik", odd_inv, couple_in)
    odd_right = mm("ij,jk->ik", odd_inv, couple_out)
    to_left = mm("ij,jk->ik", couple_in, odd_left)
    to_right = mm("ji,jk->ik", couple_out, odd_right)
    coupling = mm("ij,jk->ik", couple_in, odd_right)
    coupling = jnp.where(position < wall_count - 1, coupling, jnp.zeros_like(coupling))
    rhs_left = mm("ji,jv->iv", odd_left, rhs_odd)
    rhs_right = mm("ji,jv->iv", odd_right, rhs_odd)
    from_left = unpack(
        lax.ppermute(
            jnp.concatenate([to_right, coupling, rhs_right], axis=1),
            "wall",
            pairs_of(range(wall_count), 1, wall_count),
        ),
        unknowns,
    )
    diag = diag_even - to_left - from_left[0]
    upper_right = coupling
    upper_left = from_left[1]
    rhs = rhs_even + rhs_left + from_left[2]

    stride = 1
    while 2 * stride < wall_count:
        inv = inverse_spd(diag)
        left = mm("ij,kj->ik", inv, upper_left)
        right = mm("ij,jk->ik", inv, upper_right)
        to_left = mm("ij,jk->ik", upper_left, left)
        to_right = mm("ji,jk->ik", upper_right, right)
        coupling = mm("ij,jk->ik", upper_left, right)
        rhs_left = mm("ji,jv->iv", left, rhs)
        rhs_right = mm("ji,jv->iv", right, rhs)
        from_right = unpack(
            lax.ppermute(
                jnp.concatenate([to_left, coupling, rhs_left], axis=1),
                "wall",
                pairs_of(range(wall_count), -stride, wall_count),
            ),
            unknowns,
        )
        from_left = unpack(
            lax.ppermute(
                jnp.concatenate([to_right, coupling, rhs_right], axis=1),
                "wall",
                pairs_of(range(wall_count), stride, wall_count),
            ),
            unknowns,
        )
        diag = diag - from_right[0] - from_left[0]
        upper_right = from_right[1]
        upper_left = from_left[1]
        rhs = rhs + from_right[2] + from_left[2]
        stride *= 2

    if stride < wall_count:
        partner_pairs = [(v, (v + stride) % wall_count) for v in range(wall_count)]
        partner = unpack2(
            lax.ppermute(jnp.concatenate([diag, rhs], axis=1), "wall", partner_pairs), unknowns
        )
        cross = upper_right + jnp.swapaxes(upper_left, 0, 1)
        pair = jnp.concatenate(
            [
                jnp.concatenate([diag, -cross], axis=1),
                jnp.concatenate([-jnp.swapaxes(cross, 0, 1), partner[0]], axis=1),
            ],
            axis=0,
        )
        pair_inv = inverse_spd(pair)
        values = mm("ij,jv->iv", pair_inv[:unknowns, :unknowns], rhs) + mm(
            "ij,jv->iv", pair_inv[:unknowns, unknowns:], partner[1]
        )
    else:
        values = mm("ij,jv->iv", inverse_spd(diag), rhs)

    next_values = lax.ppermute(values, "wall", pairs_of(range(1, wall_count), -1, wall_count))
    odd_values = (
        mm("ij,jv->iv", odd_inv, rhs_odd)
        + mm("ij,jv->iv", odd_left, values)
        + mm("ij,jv->iv", odd_right, next_values)
    )
    own = jnp.stack([values, odd_values], axis=0)
    return jnp.swapaxes(own, 1, 2)[None, None]


def solution(mesh):
    placed = (
        P("span", "stream", "wall", None, None),
        P("span", "stream", "wall", None, None),
        P(),
        P(),
        P(),
        P("span", "stream", "wall"),
        P("span", "stream", "wall", None),
        P("span", "stream", "wall", None),
    )
    return jax.shard_map(
        on_device,
        mesh=mesh,
        in_specs=placed,
        out_specs=P("span", "stream", "wall", None, None),
        check_vma=False,
    )
```
